256 devices in a mesh: row: 4 (over y), col: 64 (over x, z, core).
Axes of the slice: x: 4, y: 4, z: 8, core: 2. Of those that a mesh axis runs over, the one named last changes fastest.
Arguments:
- features: bfloat16 [2097152, 128], P(('row', 'col')), may hold values from -6 to 6
- position: float32 [3, 2097152], P(None, ('row', 'col')), may hold values from -6 to 6
- velocity: float32 [3, 2097152], P(None, ('row', 'col')), may hold values from -6 to 6
- noise: float32 [3, 2097152], P(None, ('row', 'col')), may hold values from -6 to 6
- charge: float32 [2097152], P(('row', 'col')), may hold values from -18 to 18
- frac: float32 [3, 2097152], P(None, ('row', 'col')), may hold values from 0 to 1
- cell: int32 [3, 2097152], P(None, ('row', 'col')), may hold values from 0 to 511, as said below
- dest: int32 [2097152, 1], P(('row', 'col')), may hold values from 0 to 63; in each aligned block of 8192 rows (0 to 8191, 8192 to 16383, ...) at most 256 rows name the same one
- w_in: bfloat16 [128, 256], replicated, may hold values from -0.5 to 0.5
- w_out: bfloat16 [256, 128], replicated, may hold values from -0.375 to 0.375
- w_force: bfloat16 [3, 256], replicated, may hold values from -0.375 to 0.375
Outputs:
- arrived_feat: bfloat16 [4194304, 128], P(('row', 'col'))
- arrived_state: float32 [6, 4194304], P(None, ('row', 'col'))
- spectrum: float32 [2, 128, 512, 512], P(None, 'row', 'col')
The draws below stay inside these ranges and needn't reach their ends.
Inputs may be any that keep to these rules, and one draw needn't show every extreme that they name: For the atom held by device d, cell[0] lies in [(d // 64) * 32, (d // 64 + 1) * 32) and cell[2] in [(d % 64) * 8, (d % 64 + 1) * 8); cell[1] is any cell along y. `dest`: among the atoms of one device no value is named by more than 256 atoms, and some device names some value exactly 256 times.
All inputs are finite; a program needn't handle non-finite values.
Results may differ from the reference program's by a relative error of at most 0.0055.
Values may be sent and summed in bfloat16 or wider, within the bound.
No kernel may reach another device: no remote copies, remote signals or barrier semaphores. Data moves between devices by JAX's collectives and lax.ppermute only.
A program may use at most 128 MiB of HBM per device.

```python
import math
import jax
import jax.numpy as jnp
import numpy as np
from jax import lax

F = 128
H = 256
A_DEV = 8192
BX = 32
GY = 512
GZ = 512
ATOMS = 2097152
CAP = 256
GX = 128
BZ = 8
N_COL = 64


def draw_cell(key, part):
    ids = jnp.arange(ATOMS, dtype=jnp.int32)
    device = ids // A_DEV
    n_col = GZ // BZ
    row_ids = device // n_col
    col_ids = device % n_col
    key_x, key_y, key_z = jax.random.split(jax.random.fold_in(key, 11), 3)
    cell_x = row_ids * BX + jax.random.randint(key_x, (ATOMS,), 0, BX, dtype=jnp.int32)
    cell_y = jax.random.randint(key_y, (ATOMS,), 0, GY, dtype=jnp.int32)
    cell_z = col_ids * BZ + jax.random.randint(key_z, (ATOMS,), 0, BZ, dtype=jnp.int32)
    return jnp.stack([cell_x, cell_y, cell_z]).astype(jnp.int32)


def block_scale(own_key, shape, cuts, smallest, top_value):
    gain = 1.0
    for axis_at, shards_of in cuts:
        steps = jax.random.uniform(jax.random.fold_in(jax.random.fold_in(own_key, 6), axis_at), (shards_of,), jnp.float32, smallest / len(cuts), top_value / len(cuts))
        gain = gain * jnp.repeat(jnp.exp(steps), shape[axis_at] // shards_of).reshape((-1,) + (1,) * (len(shape) - 1 - axis_at))
    return gain


def routed_block(rng, own, number, rows, number_of, top, most, lean):
    order = jax.random.permutation(rng, number_of)
    heavy_load, common = shares(number_of, rows * top, most, lean, True), shares(number_of, rows * top, most, lean, False)
    places = jnp.arange(number_of)

    def named(sizes, offset_by):
        used = int((sizes > 0).sum())
        fixed = max(1, used // 4)
        passed = fixed + (places - fixed + offset_by * (used - fixed)) % max(1, number_of - fixed)
        return jnp.zeros((number_of,), jnp.int32).at[order[jnp.where(places < fixed, places, passed)]].set(jnp.asarray(sizes, jnp.int32))

    sizes = jnp.where(number % 4 == 0, named(heavy_load, number // 4), named(common, number - number // 4 - 1))
    mixed = jax.random.permutation(jax.random.fold_in(own, 3), number_of)
    source_of, taker = mixed[0:number_of // 2 * 2:2], mixed[1:number_of // 2 * 2:2]
    slack = jnp.minimum(sizes[source_of] - 1, most - sizes[taker]) // 2
    slack = jnp.where((source_of == order[0]) | (taker == order[0]) | (sizes[taker] == 0), 0, jnp.maximum(slack, 0))
    passed = jax.random.randint(jax.random.fold_in(own, 4), (number_of // 2,), 0, 1 << 20) % (slack + 1)
    sizes = sizes.at[source_of].add(-passed).at[taker].add(passed)
    members = jnp.searchsorted(jnp.cumsum(sizes), jnp.arange(rows * top), side="right").astype(jnp.int32)
    table = members.reshape(top, rows).T
    table = table[jax.random.permutation(jax.random.fold_in(own, 1), rows)]
    offset_by = jax.random.randint(jax.random.fold_in(own, 2), (rows, 1), 0, top)
    return jnp.take_along_axis(table, (jnp.arange(top)[None, :] + offset_by) % top, axis=1)


def shares(count, total, bound, slope, full):
    weights = [(1 << 20) // math.isqrt(standing ** slope) + 1 for standing in range(1, count + 1)]
    largest = bound if full else min(bound, max(-(-total // count), total * weights[0] // sum(weights)))
    least = 1 if total - largest >= count - 1 else 0
    holding, rest = [largest] + [least] * (count - 1), total - largest - least * (count - 1)
    while rest > 0:
        movable = [i for i in range(1, count) if holding[i] < largest] or [i for i in range(1, count) if holding[i] < bound]
        pool, budget = sum([weights[i] for i in movable]), rest
        for i in movable:
            addition = min(bound - holding[i], max(1, budget * weights[i] // pool), rest)
            holding[i] = holding[i] + addition
            rest = rest - addition
    return np.array(holding)


def gaussian(rng, dims, spread, bound, shards=(), held_as=jnp.bfloat16):
    factor_of = block_scale(rng, dims, shards, -0.22, 0.18) if shards else 1.0
    values = jax.random.normal(rng, dims, jnp.float32) * spread * factor_of
    return jnp.minimum(jnp.maximum(values, -bound), bound).astype(held_as)


def setup_inputs(seed: int = 0) -> dict:
    key_of = jax.random.split(jax.random.key(seed), 12)
    features = gaussian(key_of[0], (ATOMS, F), 1.0, 6.0, ((0, 256),))
    position = gaussian(key_of[1], (3, ATOMS), 1.0, 6.0, ((1, 256),), jnp.float32)
    velocity = gaussian(key_of[2], (3, ATOMS), 1.0, 6.0, ((1, 256),), jnp.float32)
    noise = gaussian(key_of[3], (3, ATOMS), 1.0, 6.0, ((1, 256),), jnp.float32)
    charge = gaussian(key_of[4], (ATOMS,), 3.0, 18.0, ((0, 256),), jnp.float32)
    frac = jnp.clip(1.0 * jax.random.uniform(key_of[5], (3, ATOMS), jnp.float32) ** block_scale(key_of[5], (3, ATOMS), ((1, 256),), -0.2, 0.2), 0.0, 1.0)
    cell = draw_cell(jax.random.fold_in(key_of[11], 71), 0)
    dest_keys = jax.random.split(jax.random.fold_in(key_of[7], 1), ATOMS // A_DEV)
    dest_turns = jax.random.permutation(jax.random.fold_in(key_of[7], 3), ATOMS // A_DEV)
    dest = jax.vmap(lambda own, number: routed_block(jax.random.fold_in(key_of[7], 2), own, number, A_DEV, N_COL, 1, CAP, 1))(dest_keys, dest_turns).reshape((ATOMS, 1))
    w_in = gaussian(key_of[8], (F, H), F ** -0.5, 0.5)
    w_out = gaussian(key_of[9], (H, F), H ** -0.5, 0.375)
    w_force = gaussian(key_of[10], (3, H), H ** -0.5, 0.375)
    return {"features": features, "position": position, "velocity": velocity, "noise": noise, "charge": charge, "frac": frac, "cell": cell, "dest": dest, "w_in": w_in, "w_out": w_out, "w_force": w_force}


def bspline(u):
    u2 = u * u
    u3 = u2 * u
    w0 = (1.0 - u) * (1.0 - u) * (1.0 - u) / 6.0
    w1 = (3.0 * u3 - 6.0 * u2 + 4.0) / 6.0
    w2 = (-3.0 * u3 + 3.0 * u2 + 3.0 * u + 1.0) / 6.0
    w3 = u3 / 6.0
    return jnp.stack([w0, w1, w2, w3])

def reference(features, position, velocity, noise, charge, frac, cell, dest, w_in, w_out, w_force):
    n_dev = ATOMS // A_DEV

    def per_device(items):
        feat, pos, vel, noi, target = items
        hidden = jax.nn.silu(jnp.dot(feat, w_in, preferred_element_type=jnp.float32)).astype(jnp.bfloat16)
        new_feat = (feat.astype(jnp.float32) + jnp.dot(hidden, w_out, preferred_element_type=jnp.float32)).astype(jnp.bfloat16)
        force = lax.dot_general(w_force, hidden, (((1,), (1,)), ((), ())), preferred_element_type=jnp.float32)
        new_vel = 0.8 * vel + 0.5 * force + 0.6 * noi
        new_pos = pos + 0.5 * new_vel
        onehot = (target[:, None] == jnp.arange(N_COL, dtype=jnp.int32)[None, :]).astype(jnp.int32)
        rank = lax.optimization_barrier(jnp.sum(jnp.cumsum(onehot, axis=0) * onehot, axis=1)) - 1
        return (new_feat, jnp.concatenate([new_pos, new_vel], axis=0), rank.astype(jnp.int32))

    def split3(arr):
        return arr.reshape(3, n_dev, A_DEV).transpose(1, 0, 2)
    targets = dest[:, 0].reshape(n_dev, A_DEV)
    new_feat, state, rank = lax.map(per_device, (features.reshape(n_dev, A_DEV, F), split3(position), split3(velocity), split3(noise), targets))
    dev_ids = jnp.arange(n_dev, dtype=jnp.int32)[:, None]
    row_ids = dev_ids // N_COL
    col_ids = dev_ids % N_COL
    slot = (((row_ids * N_COL + targets) * N_COL + col_ids) * CAP + rank).reshape(-1).astype(jnp.int32)
    arrived_feat = jnp.zeros((n_dev * N_COL * CAP, F), jnp.bfloat16).at[slot].set(new_feat.reshape(-1, F))
    arrived_state = jnp.zeros((6, n_dev * N_COL * CAP), jnp.float32).at[:, slot].set(state.transpose(1, 0, 2).reshape(6, -1))
    wx = bspline(frac[0])
    wy = bspline(frac[1])
    wz = bspline(frac[2])

    def add_term(grid, k):
        kx = k // 16
        ky = k // 4 % 4
        kz = k % 4
        weight = charge * wx[kx] * wy[ky] * wz[kz]
        ix = ((cell[0] + kx) % GX).astype(jnp.int32)
        iy = ((cell[1] + ky) % GY).astype(jnp.int32)
        iz = ((cell[2] + kz) % GZ).astype(jnp.int32)
        return (grid.at[ix, iy, iz].add(weight), None)
    grid, unused = lax.scan(add_term, jnp.zeros((GX, GY, GZ), jnp.float32), jnp.arange(64, dtype=jnp.int32))
    transformed = jnp.fft.fft(grid, axis=2) / jnp.sqrt(jnp.float32(GZ))
    spectrum = jnp.stack([jnp.real(transformed), jnp.imag(transformed)]).astype(jnp.float32)
    return (arrived_feat, arrived_state, spectrum)
```

```python
import jax
import jax.numpy as jnp
from jax import lax
from jax.sharding import PartitionSpec as P

BX = 32
GY = 512
GZ = 512


def from_behind(shard, axis, by):
    count = lax.axis_size(axis)
    return lax.ppermute(shard, axis, [(i, (i + by) % count) for i in range(count)])


def bspline(u):
    u2 = u * u
    u3 = u2 * u
    w0 = (1.0 - u) * (1.0 - u) * (1.0 - u) / 6.0
    w1 = (3.0 * u3 - 6.0 * u2 + 4.0) / 6.0
    w2 = (-3.0 * u3 + 3.0 * u2 + 3.0 * u + 1.0) / 6.0
    w3 = u3 / 6.0
    return jnp.stack([w0, w1, w2, w3])


def spline_rows(base, weights, width, wrap):
    columns = jnp.arange(width, dtype=jnp.int32)[None, :]
    total = jnp.zeros((base.shape[0], width), jnp.float32)
    for shift_k in range(4):
        place = base + shift_k
        if wrap:
            place = place % width
        total = total + weights[shift_k][:, None] * (place[:, None] == columns).astype(jnp.float32)
    return total


def update_rows(feat, pos, vel, noi, w_in, w_out, w_force):
    hidden = jax.nn.silu(jnp.dot(feat, w_in, preferred_element_type=jnp.float32)).astype(
        jnp.bfloat16
    )
    new_feat = (
        feat.astype(jnp.float32) + jnp.dot(hidden, w_out, preferred_element_type=jnp.float32)
    ).astype(jnp.bfloat16)
    force = lax.dot_general(
        w_force, hidden, (((1,), (1,)), ((), ())), preferred_element_type=jnp.float32
    )
    new_vel = 0.8 * vel + 0.5 * force + 0.6 * noi
    new_pos = pos + 0.5 * new_vel
    return (new_feat, jnp.concatenate([new_pos, new_vel], axis=0))


def dest_rank(target, n_col, block):
    atoms = target.shape[0]
    groups = atoms // block
    onehot = (target[:, None] == jnp.arange(n_col, dtype=jnp.int32)[None, :]).astype(jnp.bfloat16)
    grouped = onehot.reshape(groups, block, n_col)
    lower = (
        jnp.arange(block, dtype=jnp.int32)[:, None] >= jnp.arange(block, dtype=jnp.int32)[None, :]
    ).astype(jnp.bfloat16)
    within = jnp.einsum("ij,gjd->gid", lower, grouped, preferred_element_type=jnp.float32)
    totals = within[:, block - 1, :].astype(jnp.bfloat16)
    before = (
        jnp.arange(groups, dtype=jnp.int32)[:, None] > jnp.arange(groups, dtype=jnp.int32)[None, :]
    ).astype(jnp.bfloat16)
    offsets = jnp.dot(before, totals, preferred_element_type=jnp.float32)
    counted = (within + offsets[:, None, :]) * grouped.astype(jnp.float32)
    rank = jnp.sum(counted, axis=2).reshape(atoms).astype(jnp.int32) - 1
    return onehot, rank


def body(features, position, velocity, noise, charge, frac, cell, dest, w_in, w_out, w_force):
    n_col = lax.axis_size("col")
    row_id = lax.axis_index("row")
    col_id = lax.axis_index("col")
    atoms = features.shape[0]
    width = features.shape[1]
    slots = 2 * atoms // n_col
    target = dest[:, 0]
    onehot, rank = dest_rank(target, n_col, 256)
    new_feat, state = update_rows(features, position, velocity, noise, w_in, w_out, w_force)
    slot = target * slots + rank
    feat_buf = (
        jnp.zeros((n_col * slots, width), jnp.bfloat16)
        .at[slot]
        .set(new_feat, unique_indices=True, mode="promise_in_bounds")
        .reshape(n_col, slots, width)
    )
    rank_hot = (rank[:, None] == jnp.arange(slots, dtype=jnp.int32)[None, :]).astype(jnp.bfloat16)
    state_lhs = state.astype(jnp.bfloat16)[None, :, :] * onehot.T[:, None, :]
    state_buf = jnp.dot(
        state_lhs.reshape(n_col * 6, atoms), rank_hot, preferred_element_type=jnp.float32
    ).astype(jnp.bfloat16).reshape(n_col, 6, slots)
    feat_buf, state_buf, charge, frac, cell = lax.optimization_barrier(
        (feat_buf, state_buf, charge, frac, cell)
    )
    got_feat = lax.all_to_all(feat_buf, "col", split_axis=0, concat_axis=0, tiled=True)
    planes_z = GZ // n_col
    ext_x = BX + 3
    ext_z = planes_z + 3
    local_x = cell[0] - row_id * BX
    local_y = cell[1]
    local_z = cell[2] - col_id * planes_z
    wx = bspline(frac[0])
    wy = bspline(frac[1])
    wz = bspline(frac[2])
    block = min(atoms, 2048)
    extended = jnp.zeros((ext_z * ext_x, GY), jnp.float32)
    for start in range(0, atoms, block):
        stop = start + block
        rows_x = spline_rows(local_x[start:stop], wx[:, start:stop], ext_x, False)
        rows_y = spline_rows(local_y[start:stop], wy[:, start:stop], GY, True)
        rows_z = spline_rows(local_z[start:stop], wz[:, start:stop], ext_z, False)
        kron = (
            charge[start:stop][:, None, None] * rows_z[:, :, None] * rows_x[:, None, :]
        ).reshape(block, ext_z * ext_x)
        extended = extended + lax.dot_general(
            kron,
            rows_y,
            (((0,), (0,)), ((), ())),
            precision=lax.Precision.HIGH,
            preferred_element_type=jnp.float32,
        )
    extended, got_feat, state_buf = lax.optimization_barrier((extended, got_feat, state_buf))
    got_state = lax.all_to_all(state_buf, "col", split_axis=0, concat_axis=0, tiled=True)
    arrived_feat = got_feat.reshape(n_col * slots, width)
    arrived_state = got_state.astype(jnp.float32).transpose(1, 0, 2).reshape(6, n_col * slots)
    extended = extended.reshape(ext_z, ext_x, GY)
    from_below = from_behind(extended[:, BX:, :].astype(jnp.bfloat16), "row", 1).astype(jnp.float32)
    slab = extended[:, :BX, :].at[:, :3, :].add(from_below)
    from_lower = from_behind(slab[planes_z:].astype(jnp.bfloat16), "col", 1).astype(jnp.float32)
    brick = slab[:planes_z].at[:3].add(from_lower)
    pencil = lax.all_to_all(
        brick.astype(jnp.bfloat16), "col", split_axis=2, concat_axis=0, tiled=True
    )
    table = dft_table()
    table_hi = table.astype(jnp.bfloat16)
    table_lo = (table - table_hi.astype(jnp.float32)).astype(jnp.bfloat16)
    dims = (((0,), (0,)), ((), ()))
    both = lax.dot_general(
        pencil, table_hi, dims, preferred_element_type=jnp.float32
    ) + lax.dot_general(pencil, table_lo, dims, preferred_element_type=jnp.float32)
    norm_scale = 1.0 / jnp.sqrt(jnp.float32(GZ))
    real_part = both[..., :GZ] * norm_scale
    imag_part = -both[..., GZ:] * norm_scale
    spectrum = jnp.stack([real_part, imag_part])
    return (arrived_feat, arrived_state, spectrum)


def dft_table():
    coarse = GZ // 32
    z = jnp.arange(GZ, dtype=jnp.int32)[:, None]
    step = 2.0 * jnp.pi / GZ
    hi_angle = step * ((z * (32 * jnp.arange(coarse, dtype=jnp.int32)[None, :])) % GZ).astype(jnp.float32)
    lo_angle = step * ((z * jnp.arange(32, dtype=jnp.int32)[None, :]) % GZ).astype(jnp.float32)
    ca, sa = jnp.cos(hi_angle)[:, :, None], jnp.sin(hi_angle)[:, :, None]
    cb, sb = jnp.cos(lo_angle)[:, None, :], jnp.sin(lo_angle)[:, None, :]
    cos_t = (ca * cb - sa * sb).reshape(GZ, GZ)
    sin_t = (sa * cb + ca * sb).reshape(GZ, GZ)
    return jnp.concatenate([cos_t, sin_t], axis=1)


def solution(mesh):
    in_specs = (
        P(("row", "col"), None),
        P(None, ("row", "col")),
        P(None, ("row", "col")),
        P(None, ("row", "col")),
        P(("row", "col")),
        P(None, ("row", "col")),
        P(None, ("row", "col")),
        P(("row", "col"), None),
        P(),
        P(),
        P(),
    )
    out_specs = (P(("row", "col"), None), P(None, ("row", "col")), P(None, "row", "col", None))
    return jax.shard_map(body, mesh=mesh, in_specs=in_specs, out_specs=out_specs, check_vma=False)
```

```python
import jax
import jax.numpy as jnp
from jax import lax
from jax.sharding import PartitionSpec as P

BX = 32
GY = 512
GZ = 512


def from_behind(shard, axis, by):
    count = lax.axis_size(axis)
    return lax.ppermute(shard, axis, [(i, (i + by) % count) for i in range(count)])


def bspline(u):
    u2 = u * u
    u3 = u2 * u
    w0 = (1.0 - u) * (1.0 - u) * (1.0 - u) / 6.0
    w1 = (3.0 * u3 - 6.0 * u2 + 4.0) / 6.0
    w2 = (-3.0 * u3 + 3.0 * u2 + 3.0 * u + 1.0) / 6.0
    w3 = u3 / 6.0
    return jnp.stack([w0, w1, w2, w3])


def spline_rows(base, weights, width, wrap):
    columns = jnp.arange(width, dtype=jnp.int32)[None, :]
    total = jnp.zeros((base.shape[0], width), jnp.float32)
    for shift_k in range(4):
        place = base + shift_k
        if wrap:
            place = place % width
        total = total + weights[shift_k][:, None] * (place[:, None] == columns).astype(jnp.float32)
    return total


def update_rows(feat, pos, vel, noi, w_in, w_out, w_force):
    hidden = jax.nn.silu(jnp.dot(feat, w_in, preferred_element_type=jnp.float32)).astype(
        jnp.bfloat16
    )
    new_feat = (
        feat.astype(jnp.float32) + jnp.dot(hidden, w_out, preferred_element_type=jnp.float32)
    ).astype(jnp.bfloat16)
    force = lax.dot_general(
        w_force, hidden, (((1,), (1,)), ((), ())), preferred_element_type=jnp.float32
    )
    new_vel = 0.8 * vel + 0.5 * force + 0.6 * noi
    new_pos = pos + 0.5 * new_vel
    return (new_feat, jnp.concatenate([new_pos, new_vel], axis=0))


def dest_rank(target, n_col, block):
    atoms = target.shape[0]
    groups = atoms // block
    onehot = (target[:, None] == jnp.arange(n_col, dtype=jnp.int32)[None, :]).astype(jnp.bfloat16)
    grouped = onehot.reshape(groups, block, n_col)
    lower = (
        jnp.arange(block, dtype=jnp.int32)[:, None] >= jnp.arange(block, dtype=jnp.int32)[None, :]
    ).astype(jnp.bfloat16)
    within = jnp.einsum("ij,gjd->gid", lower, grouped, preferred_element_type=jnp.float32)
    totals = within[:, block - 1, :].astype(jnp.bfloat16)
    before = (
        jnp.arange(groups, dtype=jnp.int32)[:, None] > jnp.arange(groups, dtype=jnp.int32)[None, :]
    ).astype(jnp.bfloat16)
    offsets = jnp.dot(before, totals, preferred_element_type=jnp.float32)
    counted = (within + offsets[:, None, :]) * grouped.astype(jnp.float32)
    rank = jnp.sum(counted, axis=2).reshape(atoms).astype(jnp.int32) - 1
    return onehot, rank


def body(features, position, velocity, noise, charge, frac, cell, dest, w_in, w_out, w_force):
    n_col = lax.axis_size("col")
    row_id = lax.axis_index("row")
    col_id = lax.axis_index("col")
    atoms = features.shape[0]
    width = features.shape[1]
    slots = 2 * atoms // n_col
    target = dest[:, 0]
    onehot, rank = dest_rank(target, n_col, 256)
    new_feat, state = update_rows(features, position, velocity, noise, w_in, w_out, w_force)
    slot = target * slots + rank
    feat_buf = (
        jnp.zeros((n_col * slots, width), jnp.bfloat16)
        .at[slot]
        .set(new_feat, unique_indices=True, mode="promise_in_bounds")
        .reshape(n_col, slots, width)
    )
    feat_buf, state, rank, onehot, charge, frac, cell = lax.optimization_barrier(
        (feat_buf, state, rank, onehot, charge, frac, cell)
    )
    got_feat = lax.all_to_all(feat_buf, "col", split_axis=0, concat_axis=0, tiled=True)
    rank_hot = (rank[:, None] == jnp.arange(slots, dtype=jnp.int32)[None, :]).astype(jnp.bfloat16)
    state_lhs = state.astype(jnp.bfloat16)[:, None, :] * onehot.T[None, :, :]
    state_buf = jnp.dot(
        state_lhs.reshape(6 * n_col, atoms), rank_hot, preferred_element_type=jnp.float32
    ).astype(jnp.bfloat16).reshape(6, n_col, slots)
    planes_z = GZ // n_col
    ext_x = BX + 3
    ext_z = planes_z + 3
    local_x = cell[0] - row_id * BX
    local_y = cell[1]
    local_z = cell[2] - col_id * planes_z
    wx = bspline(frac[0])
    wy = bspline(frac[1])
    wz = bspline(frac[2])
    block = min(atoms, 2048)
    extended = jnp.zeros((ext_z * ext_x, GY), jnp.float32)
    for start in range(0, atoms, block):
        stop = start + block
        rows_x = spline_rows(local_x[start:stop], wx[:, start:stop], ext_x, False)
        rows_y = spline_rows(local_y[start:stop], wy[:, start:stop], GY, True)
        rows_z = spline_rows(local_z[start:stop], wz[:, start:stop], ext_z, False)
        kron = (
            charge[start:stop][:, None, None] * rows_z[:, :, None] * rows_x[:, None, :]
        ).reshape(block, ext_z * ext_x)
        extended = extended + lax.dot_general(
            kron,
            rows_y,
            (((0,), (0,)), ((), ())),
            precision=lax.Precision.HIGH,
            preferred_element_type=jnp.float32,
        )
    extended = extended.reshape(ext_z, ext_x, GY)
    from_below = from_behind(extended[:, BX:, :].astype(jnp.bfloat16), "row", 1).astype(jnp.float32)
    slab = extended[:, :BX, :].at[:, :3, :].add(from_below)
    from_lower = from_behind(slab[planes_z:].astype(jnp.bfloat16), "col", 1).astype(jnp.float32)
    brick = slab[:planes_z].at[:3].add(from_lower).astype(jnp.bfloat16)
    brick, got_feat, state_buf = lax.optimization_barrier((brick, got_feat, state_buf))
    arrived_feat = got_feat.reshape(n_col * slots, width)
    y_block = GY // n_col
    state_part = state_buf.transpose(1, 0, 2).reshape(n_col, 6 * slots)
    grid_part = (
        brick.reshape(planes_z, BX, n_col, y_block).transpose(2, 0, 1, 3).reshape(n_col, -1)
    )
    got = lax.all_to_all(
        jnp.concatenate([state_part, grid_part], axis=1), "col", split_axis=0, concat_axis=0, tiled=True
    )
    arrived_state = (
        got[:, : 6 * slots].reshape(n_col, 6, slots).transpose(1, 0, 2).reshape(6, n_col * slots)
    ).astype(jnp.float32)
    pencil = got[:, 6 * slots :].reshape(n_col * planes_z, BX, y_block)
    table = dft_table()
    table_hi = table.astype(jnp.bfloat16)
    table_lo = (table - table_hi.astype(jnp.float32)).astype(jnp.bfloat16)
    dims = (((0,), (0,)), ((), ()))
    both = lax.dot_general(
        pencil, table_hi, dims, preferred_element_type=jnp.float32
    ) + lax.dot_general(pencil, table_lo, dims, preferred_element_type=jnp.float32)
    norm_scale = 1.0 / jnp.sqrt(jnp.float32(GZ))
    real_part = both[..., :GZ] * norm_scale
    imag_part = -both[..., GZ:] * norm_scale
    spectrum = jnp.stack([real_part, imag_part])
    return (arrived_feat, arrived_state, spectrum)


def dft_table():
    coarse = GZ // 32
    z = jnp.arange(GZ, dtype=jnp.int32)[:, None]
    step = 2.0 * jnp.pi / GZ
    hi_angle = step * ((z * (32 * jnp.arange(coarse, dtype=jnp.int32)[None, :])) % GZ).astype(jnp.float32)
    lo_angle = step * ((z * jnp.arange(32, dtype=jnp.int32)[None, :]) % GZ).astype(jnp.float32)
    ca, sa = jnp.cos(hi_angle)[:, :, None], jnp.sin(hi_angle)[:, :, None]
    cb, sb = jnp.cos(lo_angle)[:, None, :], jnp.sin(lo_angle)[:, None, :]
    cos_t = (ca * cb - sa * sb).reshape(GZ, GZ)
    sin_t = (sa * cb + ca * sb).reshape(GZ, GZ)
    return jnp.concatenate([cos_t, sin_t], axis=1)


def solution(mesh):
    in_specs = (
        P(("row", "col"), None),
        P(None, ("row", "col")),
        P(None, ("row", "col")),
        P(None, ("row", "col")),
        P(("row", "col")),
        P(None, ("row", "col")),
        P(None, ("row", "col")),
        P(("row", "col"), None),
        P(),
        P(),
        P(),
    )
    out_specs = (P(("row", "col"), None), P(None, ("row", "col")), P(None, "row", "col", None))
    return jax.shard_map(body, mesh=mesh, in_specs=in_specs, out_specs=out_specs, check_vma=False)
```

```python
import jax
import jax.numpy as jnp
from jax import lax
from jax.sharding import PartitionSpec as P

BX = 32
GY = 512
GZ = 512


def from_behind(shard, axis, by):
    count = lax.axis_size(axis)
    return lax.ppermute(shard, axis, [(i, (i + by) % count) for i in range(count)])


def bspline(u):
    u2 = u * u
    u3 = u2 * u
    w0 = (1.0 - u) * (1.0 - u) * (1.0 - u) / 6.0
    w1 = (3.0 * u3 - 6.0 * u2 + 4.0) / 6.0
    w2 = (-3.0 * u3 + 3.0 * u2 + 3.0 * u + 1.0) / 6.0
    w3 = u3 / 6.0
    return jnp.stack([w0, w1, w2, w3])


def spline_rows(base, weights, width, wrap):
    columns = jnp.arange(width, dtype=jnp.int32)[None, :]
    total = jnp.zeros((base.shape[0], width), jnp.float32)
    for shift_k in range(4):
        place = base + shift_k
        if wrap:
            place = place % width
        total = total + weights[shift_k][:, None] * (place[:, None] == columns).astype(jnp.float32)
    return total


def dest_rank(target, n_col, block):
    atoms = target.shape[0]
    groups = atoms // block
    onehot = (target[:, None] == jnp.arange(n_col, dtype=jnp.int32)[None, :]).astype(jnp.bfloat16)
    grouped = onehot.reshape(groups, block, n_col)
    lower = (
        jnp.arange(block, dtype=jnp.int32)[:, None] >= jnp.arange(block, dtype=jnp.int32)[None, :]
    ).astype(jnp.bfloat16)
    within = jnp.einsum("ij,gjd->gid", lower, grouped, preferred_element_type=jnp.float32)
    totals = within[:, block - 1, :].astype(jnp.bfloat16)
    before = (
        jnp.arange(groups, dtype=jnp.int32)[:, None] > jnp.arange(groups, dtype=jnp.int32)[None, :]
    ).astype(jnp.bfloat16)
    offsets = jnp.dot(before, totals, preferred_element_type=jnp.float32)
    counted = (within + offsets[:, None, :]) * grouped.astype(jnp.float32)
    rank = jnp.sum(counted, axis=2).reshape(atoms).astype(jnp.int32) - 1
    return onehot, rank


def body(features, position, velocity, noise, charge, frac, cell, dest, w_in, w_out, w_force):
    n_col = lax.axis_size("col")
    row_id = lax.axis_index("row")
    col_id = lax.axis_index("col")
    atoms = features.shape[0]
    width = features.shape[1]
    slots = 2 * atoms // n_col
    target = dest[:, 0]
    onehot, rank = dest_rank(target, n_col, 256)
    hidden = jax.nn.silu(jnp.dot(features, w_in, preferred_element_type=jnp.float32)).astype(
        jnp.bfloat16
    )
    new_feat = (
        features.astype(jnp.float32) + jnp.dot(hidden, w_out, preferred_element_type=jnp.float32)
    ).astype(jnp.bfloat16)
    slot = target * slots + rank
    feat_buf = (
        jnp.zeros((n_col * slots, width), jnp.bfloat16)
        .at[slot]
        .set(new_feat, unique_indices=True, mode="promise_in_bounds")
        .reshape(n_col, slots, width)
    )
    feat_buf, hidden, rank, onehot, charge, frac, cell = lax.optimization_barrier(
        (feat_buf, hidden, rank, onehot, charge, frac, cell)
    )
    got_feat = lax.all_to_all(feat_buf, "col", split_axis=0, concat_axis=0, tiled=True)
    force = lax.dot_general(
        w_force, hidden, (((1,), (1,)), ((), ())), preferred_element_type=jnp.float32
    )
    new_vel = 0.8 * velocity + 0.5 * force + 0.6 * noise
    state = jnp.concatenate([position + 0.5 * new_vel, new_vel], axis=0)
    rank_hot = (rank[:, None] == jnp.arange(slots, dtype=jnp.int32)[None, :]).astype(jnp.bfloat16)
    state_lhs = state.astype(jnp.bfloat16)[:, None, :] * onehot.T[None, :, :]
    state_buf = jnp.dot(
        state_lhs.reshape(6 * n_col, atoms), rank_hot, preferred_element_type=jnp.float32
    ).astype(jnp.bfloat16).reshape(6, n_col, slots)
    planes_z = GZ // n_col
    ext_x = BX + 3
    ext_z = planes_z + 3
    local_x = cell[0] - row_id * BX
    local_y = cell[1]
    local_z = cell[2] - col_id * planes_z
    wx = bspline(frac[0])
    wy = bspline(frac[1])
    wz = bspline(frac[2])
    block = min(atoms, 2048)
    extended = jnp.zeros((ext_z * ext_x, GY), jnp.float32)
    for start in range(0, atoms, block):
        stop = start + block
        rows_x = spline_rows(local_x[start:stop], wx[:, start:stop], ext_x, False)
        rows_y = spline_rows(local_y[start:stop], wy[:, start:stop], GY, True)
        rows_z = spline_rows(local_z[start:stop], wz[:, start:stop], ext_z, False)
        kron = (
            charge[start:stop][:, None, None] * rows_z[:, :, None] * rows_x[:, None, :]
        ).reshape(block, ext_z * ext_x)
        extended = extended + lax.dot_general(
            kron,
            rows_y,
            (((0,), (0,)), ((), ())),
            precision=lax.Precision.HIGH,
            preferred_element_type=jnp.float32,
        )
    extended = extended.reshape(ext_z, ext_x, GY)
    from_below = from_behind(extended[:, BX:, :].astype(jnp.bfloat16), "row", 1).astype(jnp.float32)
    slab = extended[:, :BX, :].at[:, :3, :].add(from_below)
    from_lower = from_behind(slab[planes_z:].astype(jnp.bfloat16), "col", 1).astype(jnp.float32)
    brick = slab[:planes_z].at[:3].add(from_lower).astype(jnp.bfloat16)
    brick, got_feat, state_buf = lax.optimization_barrier((brick, got_feat, state_buf))
    arrived_feat = got_feat.reshape(n_col * slots, width)
    y_block = GY // n_col
    state_part = state_buf.transpose(1, 0, 2).reshape(n_col, 6 * slots)
    grid_part = (
        brick.reshape(planes_z, BX, n_col, y_block).transpose(2, 0, 1, 3).reshape(n_col, -1)
    )
    got = lax.all_to_all(
        jnp.concatenate([state_part, grid_part], axis=1), "col", split_axis=0, concat_axis=0, tiled=True
    )
    arrived_state = (
        got[:, : 6 * slots].reshape(n_col, 6, slots).transpose(1, 0, 2).reshape(6, n_col * slots)
    ).astype(jnp.float32)
    pencil = got[:, 6 * slots :].reshape(n_col * planes_z, BX * y_block)
    table = dft_table()
    table_hi = table.astype(jnp.bfloat16)
    table_lo = (table - table_hi.astype(jnp.float32)).astype(jnp.bfloat16)
    dims = (((0,), (0,)), ((), ()))
    both = lax.dot_general(
        pencil, table_hi, dims, preferred_element_type=jnp.float32
    ) + lax.dot_general(pencil, table_lo, dims, preferred_element_type=jnp.float32)
    norm_scale = 1.0 / jnp.sqrt(jnp.float32(GZ))
    both = both.reshape(BX, y_block, 2 * GZ)
    real_part = both[..., :GZ] * norm_scale
    imag_part = -both[..., GZ:] * norm_scale
    spectrum = jnp.stack([real_part, imag_part])
    return (arrived_feat, arrived_state, spectrum)


def dft_table():
    coarse = GZ // 32
    z = jnp.arange(GZ, dtype=jnp.int32)[:, None]
    step = 2.0 * jnp.pi / GZ
    hi_angle = step * ((z * (32 * jnp.arange(coarse, dtype=jnp.int32)[None, :])) % GZ).astype(jnp.float32)
    lo_angle = step * ((z * jnp.arange(32, dtype=jnp.int32)[None, :]) % GZ).astype(jnp.float32)
    ca, sa = jnp.cos(hi_angle)[:, :, None], jnp.sin(hi_angle)[:, :, None]
    cb, sb = jnp.cos(lo_angle)[:, None, :], jnp.sin(lo_angle)[:, None, :]
    cos_t = (ca * cb - sa * sb).reshape(GZ, GZ)
    sin_t = (sa * cb + ca * sb).reshape(GZ, GZ)
    return jnp.concatenate([cos_t, sin_t], axis=1)


def solution(mesh):
    in_specs = (
        P(("row", "col"), None),
        P(None, ("row", "col")),
        P(None, ("row", "col")),
        P(None, ("row", "col")),
        P(("row", "col")),
        P(None, ("row", "col")),
        P(None, ("row", "col")),
        P(("row", "col"), None),
        P(),
        P(),
        P(),
    )
    out_specs = (P(("row", "col"), None), P(None, ("row", "col")), P(None, "row", "col", None))
    return jax.shard_map(body, mesh=mesh, in_specs=in_specs, out_specs=out_specs, check_vma=False)
```

```python
import jax
import jax.numpy as jnp
from jax import lax
from jax.sharding import PartitionSpec as P

BX = 32
GY = 512
GZ = 512


def from_behind(shard, axis, by):
    count = lax.axis_size(axis)
    return lax.ppermute(shard, axis, [(i, (i + by) % count) for i in range(count)])


def bspline(u):
    u2 = u * u
    u3 = u2 * u
    w0 = (1.0 - u) * (1.0 - u) * (1.0 - u) / 6.0
    w1 = (3.0 * u3 - 6.0 * u2 + 4.0) / 6.0
    w2 = (-3.0 * u3 + 3.0 * u2 + 3.0 * u + 1.0) / 6.0
    w3 = u3 / 6.0
    return jnp.stack([w0, w1, w2, w3])


def spline_rows(base, weights, width, wrap):
    columns = jnp.arange(width, dtype=jnp.int32)[None, :]
    total = jnp.zeros((base.shape[0], width), jnp.float32)
    for shift_k in range(4):
        place = base + shift_k
        if wrap:
            place = place % width
        total = total + weights[shift_k][:, None] * (place[:, None] == columns).astype(jnp.float32)
    return total


def dest_rank(target, n_col, block):
    atoms = target.shape[0]
    groups = atoms // block
    onehot = (target[:, None] == jnp.arange(n_col, dtype=jnp.int32)[None, :]).astype(jnp.bfloat16)
    grouped = onehot.reshape(groups, block, n_col)
    lower = (
        jnp.arange(block, dtype=jnp.int32)[:, None] >= jnp.arange(block, dtype=jnp.int32)[None, :]
    ).astype(jnp.bfloat16)
    within = jnp.einsum("ij,gjd->gid", lower, grouped, preferred_element_type=jnp.float32)
    totals = within[:, block - 1, :].astype(jnp.bfloat16)
    before = (
        jnp.arange(groups, dtype=jnp.int32)[:, None] > jnp.arange(groups, dtype=jnp.int32)[None, :]
    ).astype(jnp.bfloat16)
    offsets = jnp.dot(before, totals, preferred_element_type=jnp.float32)
    counted = (within + offsets[:, None, :]) * grouped.astype(jnp.float32)
    rank = jnp.sum(counted, axis=2).reshape(atoms).astype(jnp.int32) - 1
    return onehot, rank


def body(features, position, velocity, noise, charge, frac, cell, dest, w_in, w_out, w_force):
    n_col = lax.axis_size("col")
    row_id = lax.axis_index("row")
    col_id = lax.axis_index("col")
    atoms = features.shape[0]
    width = features.shape[1]
    slots = 2 * atoms // n_col
    target = dest[:, 0]
    onehot, rank = dest_rank(target, n_col, 256)
    hidden = jax.nn.silu(jnp.dot(features, w_in, preferred_element_type=jnp.float32)).astype(
        jnp.bfloat16
    )
    new_feat = (
        features.astype(jnp.float32) + jnp.dot(hidden, w_out, preferred_element_type=jnp.float32)
    ).astype(jnp.bfloat16)
    slot = target * slots + rank
    feat_buf = (
        jnp.zeros((n_col * slots, width), jnp.bfloat16)
        .at[slot]
        .set(new_feat, unique_indices=True, mode="promise_in_bounds")
        .reshape(n_col, slots, width)
    )
    feat_buf, hidden, rank, onehot, charge, frac, cell = lax.optimization_barrier(
        (feat_buf, hidden, rank, onehot, charge, frac, cell)
    )
    got_feat = lax.all_to_all(feat_buf, "col", split_axis=0, concat_axis=0, tiled=True)
    force = lax.dot_general(
        w_force, hidden, (((1,), (1,)), ((), ())), preferred_element_type=jnp.float32
    )
    new_vel = 0.8 * velocity + 0.5 * force + 0.6 * noise
    state = jnp.concatenate([position + 0.5 * new_vel, new_vel], axis=0)
    rank_hot = (rank[:, None] == jnp.arange(slots, dtype=jnp.int32)[None, :]).astype(jnp.bfloat16)
    state_lhs = state.astype(jnp.bfloat16)[:, None, :] * onehot.T[None, :, :]
    state_buf = jnp.dot(
        state_lhs.reshape(6 * n_col, atoms), rank_hot, preferred_element_type=jnp.float32
    ).astype(jnp.bfloat16).reshape(6, n_col, slots)
    planes_z = GZ // n_col
    ext_x = BX + 3
    ext_z = planes_z + 3
    local_x = cell[0] - row_id * BX
    local_y = cell[1]
    local_z = cell[2] - col_id * planes_z
    wx = bspline(frac[0])
    wy = bspline(frac[1])
    wz = bspline(frac[2])
    block = atoms
    extended = jnp.zeros((ext_z * ext_x, GY), jnp.float32)
    for start in range(0, atoms, block):
        stop = start + block
        rows_x = spline_rows(local_x[start:stop], wx[:, start:stop], ext_x, False)
        rows_y = spline_rows(local_y[start:stop], wy[:, start:stop], GY, True)
        rows_z = spline_rows(local_z[start:stop], wz[:, start:stop], ext_z, False)
        kron = (
            charge[start:stop][:, None, None] * rows_z[:, :, None] * rows_x[:, None, :]
        ).reshape(block, ext_z * ext_x)
        extended = extended + lax.dot_general(
            kron,
            rows_y,
            (((0,), (0,)), ((), ())),
            precision=lax.Precision.HIGH,
            preferred_element_type=jnp.float32,
        )
    extended = extended.reshape(ext_z, ext_x, GY)
    from_below = from_behind(extended[:, BX:, :].astype(jnp.bfloat16), "row", 1).astype(jnp.float32)
    slab = extended[:, :BX, :].at[:, :3, :].add(from_below)
    from_lower = from_behind(slab[planes_z:].astype(jnp.bfloat16), "col", 1).astype(jnp.float32)
    brick = slab[:planes_z].at[:3].add(from_lower).astype(jnp.bfloat16)
    brick, got_feat, state_buf = lax.optimization_barrier((brick, got_feat, state_buf))
    arrived_feat = got_feat.reshape(n_col * slots, width)
    y_block = GY // n_col
    state_part = state_buf.transpose(1, 0, 2).reshape(n_col, 6 * slots)
    grid_part = (
        brick.reshape(planes_z, BX, n_col, y_block).transpose(2, 0, 1, 3).reshape(n_col, -1)
    )
    got = lax.all_to_all(
        jnp.concatenate([state_part, grid_part], axis=1), "col", split_axis=0, concat_axis=0, tiled=True
    )
    arrived_state = (
        got[:, : 6 * slots].reshape(n_col, 6, slots).transpose(1, 0, 2).reshape(6, n_col * slots)
    ).astype(jnp.float32)
    pencil = got[:, 6 * slots :].reshape(n_col * planes_z, BX * y_block)
    table = dft_table()
    table_hi = table.astype(jnp.bfloat16)
    table_lo = (table - table_hi.astype(jnp.float32)).astype(jnp.bfloat16)
    dims = (((0,), (0,)), ((), ()))
    both = lax.dot_general(
        pencil, table_hi, dims, preferred_element_type=jnp.float32
    ) + lax.dot_general(pencil, table_lo, dims, preferred_element_type=jnp.float32)
    norm_scale = 1.0 / jnp.sqrt(jnp.float32(GZ))
    both = both.reshape(BX, y_block, 2 * GZ)
    real_part = both[..., :GZ] * norm_scale
    imag_part = -both[..., GZ:] * norm_scale
    spectrum = jnp.stack([real_part, imag_part])
    return (arrived_feat, arrived_state, spectrum)


def dft_table():
    coarse = GZ // 32
    z = jnp.arange(GZ, dtype=jnp.int32)[:, None]
    step = 2.0 * jnp.pi / GZ
    hi_angle = step * ((z * (32 * jnp.arange(coarse, dtype=jnp.int32)[None, :])) % GZ).astype(jnp.float32)
    lo_angle = step * ((z * jnp.arange(32, dtype=jnp.int32)[None, :]) % GZ).astype(jnp.float32)
    ca, sa = jnp.cos(hi_angle)[:, :, None], jnp.sin(hi_angle)[:, :, None]
    cb, sb = jnp.cos(lo_angle)[:, None, :], jnp.sin(lo_angle)[:, None, :]
    cos_t = (ca * cb - sa * sb).reshape(GZ, GZ)
    sin_t = (sa * cb + ca * sb).reshape(GZ, GZ)
    return jnp.concatenate([cos_t, sin_t], axis=1)


def solution(mesh):
    in_specs = (
        P(("row", "col"), None),
        P(None, ("row", "col")),
        P(None, ("row", "col")),
        P(None, ("row", "col")),
        P(("row", "col")),
        P(None, ("row", "col")),
        P(None, ("row", "col")),
        P(("row", "col"), None),
        P(),
        P(),
        P(),
    )
    out_specs = (P(("row", "col"), None), P(None, ("row", "col")), P(None, "row", "col", None))
    return jax.shard_map(body, mesh=mesh, in_specs=in_specs, out_specs=out_specs, check_vma=False)
```

```python
import jax
import jax.numpy as jnp
from jax import lax
from jax.sharding import PartitionSpec as P

BX = 32
GY = 512
GZ = 512


def from_behind(shard, axis, by):
    count = lax.axis_size(axis)
    return lax.ppermute(shard, axis, [(i, (i + by) % count) for i in range(count)])


def bspline(u):
    u2 = u * u
    u3 = u2 * u
    w0 = (1.0 - u) * (1.0 - u) * (1.0 - u) / 6.0
    w1 = (3.0 * u3 - 6.0 * u2 + 4.0) / 6.0
    w2 = (-3.0 * u3 + 3.0 * u2 + 3.0 * u + 1.0) / 6.0
    w3 = u3 / 6.0
    return jnp.stack([w0, w1, w2, w3])


def spline_rows(base, weights, width, wrap):
    columns = jnp.arange(width, dtype=jnp.int32)[None, :]
    total = jnp.zeros((base.shape[0], width), jnp.float32)
    for shift_k in range(4):
        place = base + shift_k
        if wrap:
            place = place % width
        total = total + weights[shift_k][:, None] * (place[:, None] == columns).astype(jnp.float32)
    return total


def dest_rank(target, n_col, block):
    atoms = target.shape[0]
    groups = atoms // block
    onehot = (target[:, None] == jnp.arange(n_col, dtype=jnp.int32)[None, :]).astype(jnp.bfloat16)
    grouped = onehot.reshape(groups, block, n_col)
    lower = (
        jnp.arange(block, dtype=jnp.int32)[:, None] >= jnp.arange(block, dtype=jnp.int32)[None, :]
    ).astype(jnp.bfloat16)
    within = jnp.einsum("ij,gjd->gid", lower, grouped, preferred_element_type=jnp.float32)
    totals = within[:, block - 1, :].astype(jnp.bfloat16)
    before = (
        jnp.arange(groups, dtype=jnp.int32)[:, None] > jnp.arange(groups, dtype=jnp.int32)[None, :]
    ).astype(jnp.bfloat16)
    offsets = jnp.dot(before, totals, preferred_element_type=jnp.float32)
    counted = (within + offsets[:, None, :]) * grouped.astype(jnp.float32)
    rank = jnp.sum(counted, axis=2).reshape(atoms).astype(jnp.int32) - 1
    return onehot, rank


def feature_hidden(feat, w_in):
    return jax.nn.silu(jnp.dot(feat, w_in, preferred_element_type=jnp.float32)).astype(jnp.bfloat16)


def body(features, position, velocity, noise, charge, frac, cell, dest, w_in, w_out, w_force):
    n_col = lax.axis_size("col")
    row_id = lax.axis_index("row")
    col_id = lax.axis_index("col")
    atoms = features.shape[0]
    width = features.shape[1]
    slots = 2 * atoms // n_col
    target = dest[:, 0]
    onehot, rank = dest_rank(target, n_col, 256)
    slot = target * slots + rank
    feat_buf = (
        jnp.zeros((n_col * slots, width), jnp.bfloat16)
        .at[slot]
        .set(features, unique_indices=True, mode="promise_in_bounds")
        .reshape(n_col, slots, width)
    )
    feat_buf, features, rank, onehot, charge, frac, cell = lax.optimization_barrier(
        (feat_buf, features, rank, onehot, charge, frac, cell)
    )
    got_feat = lax.all_to_all(feat_buf, "col", split_axis=0, concat_axis=0, tiled=True)
    hidden = feature_hidden(features, w_in)
    force = lax.dot_general(
        w_force, hidden, (((1,), (1,)), ((), ())), preferred_element_type=jnp.float32
    )
    new_vel = 0.8 * velocity + 0.5 * force + 0.6 * noise
    state = jnp.concatenate([position + 0.5 * new_vel, new_vel], axis=0)
    rank_hot = (rank[:, None] == jnp.arange(slots, dtype=jnp.int32)[None, :]).astype(jnp.bfloat16)
    state_lhs = state.astype(jnp.bfloat16)[:, None, :] * onehot.T[None, :, :]
    state_buf = jnp.dot(
        state_lhs.reshape(6 * n_col, atoms), rank_hot, preferred_element_type=jnp.float32
    ).astype(jnp.bfloat16).reshape(6, n_col, slots)
    planes_z = GZ // n_col
    ext_x = BX + 3
    ext_z = planes_z + 3
    local_x = cell[0] - row_id * BX
    local_y = cell[1]
    local_z = cell[2] - col_id * planes_z
    wx = bspline(frac[0])
    wy = bspline(frac[1])
    wz = bspline(frac[2])
    block = atoms
    extended = jnp.zeros((ext_z * ext_x, GY), jnp.float32)
    for start in range(0, atoms, block):
        stop = start + block
        rows_x = spline_rows(local_x[start:stop], wx[:, start:stop], ext_x, False)
        rows_y = spline_rows(local_y[start:stop], wy[:, start:stop], GY, True)
        rows_z = spline_rows(local_z[start:stop], wz[:, start:stop], ext_z, False)
        kron = (
            charge[start:stop][:, None, None] * rows_z[:, :, None] * rows_x[:, None, :]
        ).reshape(block, ext_z * ext_x)
        extended = extended + lax.dot_general(
            kron,
            rows_y,
            (((0,), (0,)), ((), ())),
            precision=lax.Precision.HIGH,
            preferred_element_type=jnp.float32,
        )
    extended = extended.reshape(ext_z, ext_x, GY)
    from_below = from_behind(extended[:, BX:, :].astype(jnp.bfloat16), "row", 1).astype(jnp.float32)
    slab = extended[:, :BX, :].at[:, :3, :].add(from_below)
    from_lower = from_behind(slab[planes_z:].astype(jnp.bfloat16), "col", 1).astype(jnp.float32)
    brick = slab[:planes_z].at[:3].add(from_lower).astype(jnp.bfloat16)
    y_block = GY // n_col
    state_part = state_buf.transpose(1, 0, 2).reshape(n_col, 6 * slots)
    grid_part = (
        brick.reshape(planes_z, BX, n_col, y_block).transpose(2, 0, 1, 3).reshape(n_col, -1)
    )
    send = jnp.concatenate([state_part, grid_part], axis=1)
    send, got_feat = lax.optimization_barrier((send, got_feat))
    got = lax.all_to_all(send, "col", split_axis=0, concat_axis=0, tiled=True)
    arrived = got_feat.reshape(n_col * slots, width)
    arrived_hidden = feature_hidden(arrived, w_in)
    arrived_feat = (
        arrived.astype(jnp.float32)
        + jnp.dot(arrived_hidden, w_out, preferred_element_type=jnp.float32)
    ).astype(jnp.bfloat16)
    arrived_state = (
        got[:, : 6 * slots].reshape(n_col, 6, slots).transpose(1, 0, 2).reshape(6, n_col * slots)
    ).astype(jnp.float32)
    pencil = got[:, 6 * slots :].reshape(n_col * planes_z, BX * y_block)
    table = dft_table()
    table_hi = table.astype(jnp.bfloat16)
    table_lo = (table - table_hi.astype(jnp.float32)).astype(jnp.bfloat16)
    dims = (((0,), (0,)), ((), ()))
    both = lax.dot_general(
        pencil, table_hi, dims, preferred_element_type=jnp.float32
    ) + lax.dot_general(pencil, table_lo, dims, preferred_element_type=jnp.float32)
    norm_scale = 1.0 / jnp.sqrt(jnp.float32(GZ))
    both = both.reshape(BX, y_block, 2 * GZ)
    real_part = both[..., :GZ] * norm_scale
    imag_part = -both[..., GZ:] * norm_scale
    spectrum = jnp.stack([real_part, imag_part])
    return (arrived_feat, arrived_state, spectrum)


def dft_table():
    coarse = GZ // 32
    z = jnp.arange(GZ, dtype=jnp.int32)[:, None]
    step = 2.0 * jnp.pi / GZ
    hi_angle = step * ((z * (32 * jnp.arange(coarse, dtype=jnp.int32)[None, :])) % GZ).astype(jnp.float32)
    lo_angle = step * ((z * jnp.arange(32, dtype=jnp.int32)[None, :]) % GZ).astype(jnp.float32)
    ca, sa = jnp.cos(hi_angle)[:, :, None], jnp.sin(hi_angle)[:, :, None]
    cb, sb = jnp.cos(lo_angle)[:, None, :], jnp.sin(lo_angle)[:, None, :]
    cos_t = (ca * cb - sa * sb).reshape(GZ, GZ)
    sin_t = (sa * cb + ca * sb).reshape(GZ, GZ)
    return jnp.concatenate([cos_t, sin_t], axis=1)


def solution(mesh):
    in_specs = (
        P(("row", "col"), None),
        P(None, ("row", "col")),
        P(None, ("row", "col")),
        P(None, ("row", "col")),
        P(("row", "col")),
        P(None, ("row", "col")),
        P(None, ("row", "col")),
        P(("row", "col"), None),
        P(),
        P(),
        P(),
    )
    out_specs = (P(("row", "col"), None), P(None, ("row", "col")), P(None, "row", "col", None))
    return jax.shard_map(body, mesh=mesh, in_specs=in_specs, out_specs=out_specs, check_vma=False)
```

```python
import jax
import jax.numpy as jnp
from jax import lax
from jax.sharding import PartitionSpec as P

BX = 32
GY = 512
GZ = 512


def from_behind(shard, axis, by):
    count = lax.axis_size(axis)
    return lax.ppermute(shard, axis, [(i, (i + by) % count) for i in range(count)])


def bspline(u):
    u2 = u * u
    u3 = u2 * u
    w0 = (1.0 - u) * (1.0 - u) * (1.0 - u) / 6.0
    w1 = (3.0 * u3 - 6.0 * u2 + 4.0) / 6.0
    w2 = (-3.0 * u3 + 3.0 * u2 + 3.0 * u + 1.0) / 6.0
    w3 = u3 / 6.0
    return jnp.stack([w0, w1, w2, w3])


def spline_rows(base, weights, width, wrap):
    columns = jnp.arange(width, dtype=jnp.int32)[None, :]
    total = jnp.zeros((base.shape[0], width), jnp.float32)
    for shift_k in range(4):
        place = base + shift_k
        if wrap:
            place = place % width
        total = total + weights[shift_k][:, None] * (place[:, None] == columns).astype(jnp.float32)
    return total


def dest_rank(target, n_col, block):
    atoms = target.shape[0]
    groups = atoms // block
    onehot = (target[:, None] == jnp.arange(n_col, dtype=jnp.int32)[None, :]).astype(jnp.bfloat16)
    grouped = onehot.reshape(groups, block, n_col)
    lower = (
        jnp.arange(block, dtype=jnp.int32)[:, None] >= jnp.arange(block, dtype=jnp.int32)[None, :]
    ).astype(jnp.bfloat16)
    within = jnp.einsum("ij,gjd->gid", lower, grouped, preferred_element_type=jnp.float32)
    totals = within[:, block - 1, :].astype(jnp.bfloat16)
    before = (
        jnp.arange(groups, dtype=jnp.int32)[:, None] > jnp.arange(groups, dtype=jnp.int32)[None, :]
    ).astype(jnp.bfloat16)
    offsets = jnp.dot(before, totals, preferred_element_type=jnp.float32)
    counted = (within + offsets[:, None, :]) * grouped.astype(jnp.float32)
    rank = jnp.sum(counted, axis=2).reshape(atoms).astype(jnp.int32) - 1
    return onehot, rank


def feature_hidden(feat, w_in):
    return jax.nn.silu(jnp.dot(feat, w_in, preferred_element_type=jnp.float32)).astype(jnp.bfloat16)


def body(features, position, velocity, noise, charge, frac, cell, dest, w_in, w_out, w_force):
    n_col = lax.axis_size("col")
    row_id = lax.axis_index("row")
    col_id = lax.axis_index("col")
    atoms = features.shape[0]
    width = features.shape[1]
    slots = 2 * atoms // n_col
    target = dest[:, 0]
    onehot, rank = dest_rank(target, n_col, 256)
    slot = target * slots + rank
    feat_buf = (
        jnp.zeros((n_col * slots, width), jnp.bfloat16)
        .at[slot]
        .set(features, unique_indices=True, mode="promise_in_bounds")
        .reshape(n_col, slots, width)
    )
    feat_buf, features, rank, onehot, charge, frac, cell = lax.optimization_barrier(
        (feat_buf, features, rank, onehot, charge, frac, cell)
    )
    got_feat = lax.all_to_all(feat_buf, "col", split_axis=0, concat_axis=0, tiled=True)
    hidden = feature_hidden(features, w_in)
    force = lax.dot_general(
        w_force, hidden, (((1,), (1,)), ((), ())), preferred_element_type=jnp.float32
    )
    new_vel = 0.8 * velocity + 0.5 * force + 0.6 * noise
    state = jnp.concatenate([position + 0.5 * new_vel, new_vel], axis=0)
    rank_hot = (rank[:, None] == jnp.arange(slots, dtype=jnp.int32)[None, :]).astype(jnp.bfloat16)
    state_lhs = state.astype(jnp.bfloat16)[:, None, :] * onehot.T[None, :, :]
    state_buf = jnp.dot(
        state_lhs.reshape(6 * n_col, atoms), rank_hot, preferred_element_type=jnp.float32
    ).astype(jnp.bfloat16).reshape(6, n_col, slots)
    planes_z = GZ // n_col
    ext_x = BX + 3
    ext_z = planes_z + 3
    local_x = cell[0] - row_id * BX
    local_y = cell[1]
    local_z = cell[2] - col_id * planes_z
    wx = bspline(frac[0])
    wy = bspline(frac[1])
    wz = bspline(frac[2])
    block = atoms
    extended = jnp.zeros((ext_z * ext_x, GY), jnp.float32)
    for start in range(0, atoms, block):
        stop = start + block
        rows_x = spline_rows(local_x[start:stop], wx[:, start:stop], ext_x, False)
        rows_y = spline_rows(local_y[start:stop], wy[:, start:stop], GY, True)
        rows_z = spline_rows(local_z[start:stop], wz[:, start:stop], ext_z, False)
        kron = (
            charge[start:stop][:, None, None] * rows_z[:, :, None] * rows_x[:, None, :]
        ).reshape(block, ext_z * ext_x)
        extended = extended + lax.dot_general(
            kron,
            rows_y,
            (((0,), (0,)), ((), ())),
            precision=lax.Precision.HIGH,
            preferred_element_type=jnp.float32,
        )
    extended = extended.reshape(ext_z, ext_x, GY)
    from_below = from_behind(extended[:, BX:, :].astype(jnp.bfloat16), "row", 1).astype(jnp.float32)
    slab = extended[:, :BX, :].at[:, :3, :].add(from_below)
    brick = slab.astype(jnp.bfloat16)
    y_block = GY // n_col
    state_part = state_buf.transpose(1, 0, 2).reshape(n_col, 6 * slots)
    grid_part = (
        brick.reshape(ext_z, BX, n_col, y_block).transpose(2, 0, 1, 3).reshape(n_col, -1)
    )
    send = jnp.concatenate([state_part, grid_part], axis=1)
    send, got_feat = lax.optimization_barrier((send, got_feat))
    got = lax.all_to_all(send, "col", split_axis=0, concat_axis=0, tiled=True)
    arrived = got_feat.reshape(n_col * slots, width)
    arrived_hidden = feature_hidden(arrived, w_in)
    arrived_feat = (
        arrived.astype(jnp.float32)
        + jnp.dot(arrived_hidden, w_out, preferred_element_type=jnp.float32)
    ).astype(jnp.bfloat16)
    arrived_state = (
        got[:, : 6 * slots].reshape(n_col, 6, slots).transpose(1, 0, 2).reshape(6, n_col * slots)
    ).astype(jnp.float32)
    planes = got[:, 6 * slots :].reshape(n_col, ext_z, BX * y_block).astype(jnp.float32)
    spill = jnp.roll(planes[:, planes_z:], 1, axis=0)
    pencil = (
        planes[:, :planes_z].at[:, :3].add(spill).astype(jnp.bfloat16).reshape(GZ, BX * y_block)
    )
    table = dft_table()
    table_hi = table.astype(jnp.bfloat16)
    table_lo = (table - table_hi.astype(jnp.float32)).astype(jnp.bfloat16)
    dims = (((0,), (0,)), ((), ()))
    both = lax.dot_general(
        pencil, table_hi, dims, preferred_element_type=jnp.float32
    ) + lax.dot_general(pencil, table_lo, dims, preferred_element_type=jnp.float32)
    norm_scale = 1.0 / jnp.sqrt(jnp.float32(GZ))
    both = both.reshape(BX, y_block, 2 * GZ)
    real_part = both[..., :GZ] * norm_scale
    imag_part = -both[..., GZ:] * norm_scale
    spectrum = jnp.stack([real_part, imag_part])
    return (arrived_feat, arrived_state, spectrum)


def dft_table():
    coarse = GZ // 32
    z = jnp.arange(GZ, dtype=jnp.int32)[:, None]
    step = 2.0 * jnp.pi / GZ
    hi_angle = step * ((z * (32 * jnp.arange(coarse, dtype=jnp.int32)[None, :])) % GZ).astype(jnp.float32)
    lo_angle = step * ((z * jnp.arange(32, dtype=jnp.int32)[None, :]) % GZ).astype(jnp.float32)
    ca, sa = jnp.cos(hi_angle)[:, :, None], jnp.sin(hi_angle)[:, :, None]
    cb, sb = jnp.cos(lo_angle)[:, None, :], jnp.sin(lo_angle)[:, None, :]
    cos_t = (ca * cb - sa * sb).reshape(GZ, GZ)
    sin_t = (sa * cb + ca * sb).reshape(GZ, GZ)
    return jnp.concatenate([cos_t, sin_t], axis=1)


def solution(mesh):
    in_specs = (
        P(("row", "col"), None),
        P(None, ("row", "col")),
        P(None, ("row", "col")),
        P(None, ("row", "col")),
        P(("row", "col")),
        P(None, ("row", "col")),
        P(None, ("row", "col")),
        P(("row", "col"), None),
        P(),
        P(),
        P(),
    )
    out_specs = (P(("row", "col"), None), P(None, ("row", "col")), P(None, "row", "col", None))
    return jax.shard_map(body, mesh=mesh, in_specs=in_specs, out_specs=out_specs, check_vma=False)
```

```python
import jax
import jax.numpy as jnp
from jax import lax
from jax.sharding import PartitionSpec as P

BX = 32
GY = 512
GZ = 512


def from_behind(shard, axis, by):
    count = lax.axis_size(axis)
    return lax.ppermute(shard, axis, [(i, (i + by) % count) for i in range(count)])


def bspline(u):
    u2 = u * u
    u3 = u2 * u
    w0 = (1.0 - u) * (1.0 - u) * (1.0 - u) / 6.0
    w1 = (3.0 * u3 - 6.0 * u2 + 4.0) / 6.0
    w2 = (-3.0 * u3 + 3.0 * u2 + 3.0 * u + 1.0) / 6.0
    w3 = u3 / 6.0
    return jnp.stack([w0, w1, w2, w3])


def spline_rows(base, weights, width, wrap):
    columns = jnp.arange(width, dtype=jnp.int32)[None, :]
    total = jnp.zeros((base.shape[0], width), jnp.float32)
    for shift_k in range(4):
        place = base + shift_k
        if wrap:
            place = place % width
        total = total + weights[shift_k][:, None] * (place[:, None] == columns).astype(jnp.float32)
    return total


def dest_rank(target, n_col, block):
    atoms = target.shape[0]
    groups = atoms // block
    onehot = (target[:, None] == jnp.arange(n_col, dtype=jnp.int32)[None, :]).astype(jnp.bfloat16)
    grouped = onehot.reshape(groups, block, n_col)
    lower = (
        jnp.arange(block, dtype=jnp.int32)[:, None] >= jnp.arange(block, dtype=jnp.int32)[None, :]
    ).astype(jnp.bfloat16)
    within = jnp.einsum("ij,gjd->gid", lower, grouped, preferred_element_type=jnp.float32)
    totals = within[:, block - 1, :].astype(jnp.bfloat16)
    before = (
        jnp.arange(groups, dtype=jnp.int32)[:, None] > jnp.arange(groups, dtype=jnp.int32)[None, :]
    ).astype(jnp.bfloat16)
    offsets = jnp.dot(before, totals, preferred_element_type=jnp.float32)
    counted = (within + offsets[:, None, :]) * grouped.astype(jnp.float32)
    rank = jnp.sum(counted, axis=2).reshape(atoms).astype(jnp.int32) - 1
    return onehot, rank


def feature_hidden(feat, w_in):
    return jax.nn.silu(jnp.dot(feat, w_in, preferred_element_type=jnp.float32)).astype(jnp.bfloat16)


def body(features, position, velocity, noise, charge, frac, cell, dest, w_in, w_out, w_force):
    n_col = lax.axis_size("col")
    row_id = lax.axis_index("row")
    col_id = lax.axis_index("col")
    atoms = features.shape[0]
    width = features.shape[1]
    slots = 2 * atoms // n_col
    target = dest[:, 0]
    onehot, rank = dest_rank(target, n_col, 256)
    slot = target * slots + rank
    feat_buf = (
        jnp.zeros((n_col * slots, width), jnp.bfloat16)
        .at[slot]
        .set(features, unique_indices=True, mode="promise_in_bounds")
        .reshape(n_col, slots, width)
    )
    feat_buf, features, rank, onehot, charge, frac, cell = lax.optimization_barrier(
        (feat_buf, features, rank, onehot, charge, frac, cell)
    )
    got_feat = lax.all_to_all(feat_buf, "col", split_axis=0, concat_axis=0, tiled=True)
    hidden = feature_hidden(features, w_in)
    force = lax.dot_general(
        w_force, hidden, (((1,), (1,)), ((), ())), preferred_element_type=jnp.float32
    )
    new_vel = 0.8 * velocity + 0.5 * force + 0.6 * noise
    state = jnp.concatenate([position + 0.5 * new_vel, new_vel], axis=0)
    rank_hot = (rank[:, None] == jnp.arange(slots, dtype=jnp.int32)[None, :]).astype(jnp.bfloat16)
    state_lhs = state.astype(jnp.bfloat16)[:, None, :] * onehot.T[None, :, :]
    state_buf = jnp.dot(
        state_lhs.reshape(6 * n_col, atoms), rank_hot, preferred_element_type=jnp.float32
    ).astype(jnp.bfloat16).reshape(6, n_col, slots)
    planes_z = GZ // n_col
    ext_x = BX + 3
    ext_z = planes_z + 3
    local_x = cell[0] - row_id * BX
    local_y = cell[1]
    local_z = cell[2] - col_id * planes_z
    wx = bspline(frac[0])
    wy = bspline(frac[1])
    wz = bspline(frac[2])
    block = atoms
    extended = jnp.zeros((ext_z * ext_x, GY), jnp.float32)
    for start in range(0, atoms, block):
        stop = start + block
        rows_x = spline_rows(local_x[start:stop], wx[:, start:stop], ext_x, False)
        rows_y = spline_rows(local_y[start:stop], wy[:, start:stop], GY, True)
        rows_z = spline_rows(local_z[start:stop], wz[:, start:stop], ext_z, False)
        kron = (
            charge[start:stop][:, None, None] * rows_z[:, :, None] * rows_x[:, None, :]
        ).reshape(block, ext_z * ext_x)
        extended = extended + lax.dot_general(
            kron,
            rows_y,
            (((0,), (0,)), ((), ())),
            precision=lax.Precision.HIGH,
            preferred_element_type=jnp.float32,
        )
    extended = extended.reshape(ext_z, ext_x, GY)
    from_below = from_behind(extended[:, BX:, :].astype(jnp.bfloat16), "row", 1).astype(jnp.float32)
    slab = extended[:, :BX, :].at[:, :3, :].add(from_below)
    brick = slab.astype(jnp.bfloat16)
    y_block = GY // n_col
    state_part = state_buf.transpose(1, 0, 2).reshape(n_col, 6 * slots)
    grid_part = (
        brick.reshape(ext_z, BX, n_col, y_block).transpose(2, 0, 1, 3).reshape(n_col, -1)
    )
    send = jnp.concatenate([state_part, grid_part], axis=1).reshape(n_col, 2, -1)
    send, got_feat = lax.optimization_barrier((send, got_feat))
    got = lax.all_to_all(send, "col", split_axis=0, concat_axis=0, tiled=True).reshape(n_col, -1)
    arrived = got_feat.reshape(n_col * slots, width)
    arrived_hidden = feature_hidden(arrived, w_in)
    arrived_feat = (
        arrived.astype(jnp.float32)
        + jnp.dot(arrived_hidden, w_out, preferred_element_type=jnp.float32)
    ).astype(jnp.bfloat16)
    arrived_state = (
        got[:, : 6 * slots].reshape(n_col, 6, slots).transpose(1, 0, 2).reshape(6, n_col * slots)
    ).astype(jnp.float32)
    planes = got[:, 6 * slots :].reshape(n_col, ext_z, BX * y_block)
    spill = jnp.roll(planes[:, planes_z:], 1, axis=0).astype(jnp.float32)
    top = (planes[:, :3].astype(jnp.float32) + spill).astype(jnp.bfloat16)
    pencil = jnp.concatenate([top, planes[:, 3:planes_z]], axis=1).reshape(GZ, BX * y_block)
    table = dft_table()
    table_hi = table.astype(jnp.bfloat16)
    table_lo = (table - table_hi.astype(jnp.float32)).astype(jnp.bfloat16)
    dims = (((0,), (0,)), ((), ()))
    both = lax.dot_general(
        pencil, table_hi, dims, preferred_element_type=jnp.float32
    ) + lax.dot_general(pencil, table_lo, dims, preferred_element_type=jnp.float32)
    norm_scale = 1.0 / jnp.sqrt(jnp.float32(GZ))
    both = both.reshape(BX, y_block, 2 * GZ)
    real_part = both[..., :GZ] * norm_scale
    imag_part = -both[..., GZ:] * norm_scale
    spectrum = jnp.stack([real_part, imag_part])
    return (arrived_feat, arrived_state, spectrum)


def dft_table():
    coarse = GZ // 32
    z = jnp.arange(GZ, dtype=jnp.int32)[:, None]
    step = 2.0 * jnp.pi / GZ
    hi_angle = step * ((z * (32 * jnp.arange(coarse, dtype=jnp.int32)[None, :])) % GZ).astype(jnp.float32)
    lo_angle = step * ((z * jnp.arange(32, dtype=jnp.int32)[None, :]) % GZ).astype(jnp.float32)
    ca, sa = jnp.cos(hi_angle)[:, :, None], jnp.sin(hi_angle)[:, :, None]
    cb, sb = jnp.cos(lo_angle)[:, None, :], jnp.sin(lo_angle)[:, None, :]
    cos_t = (ca * cb - sa * sb).reshape(GZ, GZ)
    sin_t = (sa * cb + ca * sb).reshape(GZ, GZ)
    return jnp.concatenate([cos_t, sin_t], axis=1)


def solution(mesh):
    in_specs = (
        P(("row", "col"), None),
        P(None, ("row", "col")),
        P(None, ("row", "col")),
        P(None, ("row", "col")),
        P(("row", "col")),
        P(None, ("row", "col")),
        P(None, ("row", "col")),
        P(("row", "col"), None),
        P(),
        P(),
        P(),
    )
    out_specs = (P(("row", "col"), None), P(None, ("row", "col")), P(None, "row", "col", None))
    return jax.shard_map(body, mesh=mesh, in_specs=in_specs, out_specs=out_specs, check_vma=False)
```

```python
import jax
import jax.numpy as jnp
from jax import lax
from jax.sharding import PartitionSpec as P

BX = 32
GY = 512
GZ = 512


def from_behind(shard, axis, by):
    count = lax.axis_size(axis)
    return lax.ppermute(shard, axis, [(i, (i + by) % count) for i in range(count)])


def bspline(u):
    u2 = u * u
    u3 = u2 * u
    w0 = (1.0 - u) * (1.0 - u) * (1.0 - u) / 6.0
    w1 = (3.0 * u3 - 6.0 * u2 + 4.0) / 6.0
    w2 = (-3.0 * u3 + 3.0 * u2 + 3.0 * u + 1.0) / 6.0
    w3 = u3 / 6.0
    return jnp.stack([w0, w1, w2, w3])


def spline_rows(base, weights, width, wrap):
    columns = jnp.arange(width, dtype=jnp.int32)[None, :]
    total = jnp.zeros((base.shape[0], width), jnp.float32)
    for shift_k in range(4):
        place = base + shift_k
        if wrap:
            place = place % width
        total = total + weights[shift_k][:, None] * (place[:, None] == columns).astype(jnp.float32)
    return total


def dest_rank(target, n_col, block):
    atoms = target.shape[0]
    groups = atoms // block
    onehot = (target[:, None] == jnp.arange(n_col, dtype=jnp.int32)[None, :]).astype(jnp.bfloat16)
    grouped = onehot.reshape(groups, block, n_col)
    lower = (
        jnp.arange(block, dtype=jnp.int32)[:, None] >= jnp.arange(block, dtype=jnp.int32)[None, :]
    ).astype(jnp.bfloat16)
    within = jnp.einsum("ij,gjd->gid", lower, grouped, preferred_element_type=jnp.float32)
    totals = within[:, block - 1, :].astype(jnp.bfloat16)
    before = (
        jnp.arange(groups, dtype=jnp.int32)[:, None] > jnp.arange(groups, dtype=jnp.int32)[None, :]
    ).astype(jnp.bfloat16)
    offsets = jnp.dot(before, totals, preferred_element_type=jnp.float32)
    counted = (within + offsets[:, None, :]) * grouped.astype(jnp.float32)
    rank = jnp.sum(counted, axis=2).reshape(atoms).astype(jnp.int32) - 1
    return onehot, rank


def feature_hidden(feat, w_in):
    return jax.nn.silu(jnp.dot(feat, w_in, preferred_element_type=jnp.float32)).astype(jnp.bfloat16)


def body(features, position, velocity, noise, charge, frac, cell, dest, w_in, w_out, w_force):
    n_col = lax.axis_size("col")
    row_id = lax.axis_index("row")
    col_id = lax.axis_index("col")
    atoms = features.shape[0]
    width = features.shape[1]
    slots = 2 * atoms // n_col
    target = dest[:, 0]
    onehot, rank = dest_rank(target, n_col, 256)
    slot = target * slots + rank
    feat_buf = (
        jnp.zeros((n_col * slots, width), jnp.bfloat16)
        .at[slot]
        .set(features, unique_indices=True, mode="promise_in_bounds")
        .reshape(n_col, slots, width)
    )
    feat_buf, features, rank, onehot, charge, frac, cell = lax.optimization_barrier(
        (feat_buf, features, rank, onehot, charge, frac, cell)
    )
    got_feat = lax.all_to_all(feat_buf, "col", split_axis=0, concat_axis=0, tiled=True)
    hidden = feature_hidden(features, w_in)
    force = lax.dot_general(
        w_force, hidden, (((1,), (1,)), ((), ())), preferred_element_type=jnp.float32
    )
    new_vel = 0.8 * velocity + 0.5 * force + 0.6 * noise
    state = jnp.concatenate([position + 0.5 * new_vel, new_vel], axis=0)
    rank_hot = (rank[:, None] == jnp.arange(slots, dtype=jnp.int32)[None, :]).astype(jnp.bfloat16)
    state_lhs = state.astype(jnp.bfloat16)[:, None, :] * onehot.T[None, :, :]
    state_buf = jnp.dot(
        state_lhs.reshape(6 * n_col, atoms), rank_hot, preferred_element_type=jnp.float32
    ).astype(jnp.bfloat16).reshape(6, n_col, slots)
    planes_z = GZ // n_col
    ext_x = BX + 3
    ext_z = planes_z + 3
    local_x = cell[0] - row_id * BX
    local_y = cell[1]
    local_z = cell[2] - col_id * planes_z
    wx = bspline(frac[0])
    wy = bspline(frac[1])
    wz = bspline(frac[2])
    block = atoms
    extended = jnp.zeros((ext_z * ext_x, GY), jnp.float32)
    for start in range(0, atoms, block):
        stop = start + block
        rows_x = spline_rows(local_x[start:stop], wx[:, start:stop], ext_x, False)
        rows_y = spline_rows(local_y[start:stop], wy[:, start:stop], GY, True)
        rows_z = spline_rows(local_z[start:stop], wz[:, start:stop], ext_z, False)
        kron = (
            charge[start:stop][:, None, None] * rows_z[:, :, None] * rows_x[:, None, :]
        ).reshape(block, ext_z * ext_x)
        extended = extended + lax.dot_general(
            kron,
            rows_y,
            (((0,), (0,)), ((), ())),
            precision=lax.Precision.HIGH,
            preferred_element_type=jnp.float32,
        )
    extended = extended.reshape(ext_z, ext_x, GY)
    from_below = from_behind(extended[:, BX:, :].astype(jnp.bfloat16), "row", 1).astype(jnp.float32)
    slab = extended[:, :BX, :].at[:, :3, :].add(from_below)
    brick = slab.astype(jnp.bfloat16)
    y_block = GY // n_col
    state_part = state_buf.transpose(1, 0, 2).reshape(n_col, 6 * slots)
    grid_part = (
        brick.reshape(ext_z, BX, n_col, y_block).transpose(2, 0, 1, 3).reshape(n_col, -1)
    )
    send = jnp.concatenate([state_part, grid_part], axis=1).reshape(n_col, 2, -1)
    send, got_feat = lax.optimization_barrier((send, got_feat))
    got = lax.all_to_all(send, "col", split_axis=0, concat_axis=0, tiled=True).reshape(n_col, -1)
    arrived = got_feat.reshape(n_col * slots, width)
    arrived_hidden = feature_hidden(arrived, w_in)
    arrived_feat = (
        arrived.astype(jnp.float32)
        + jnp.dot(arrived_hidden, w_out, preferred_element_type=jnp.float32)
    ).astype(jnp.bfloat16)
    arrived_state = (
        got[:, : 6 * slots].reshape(n_col, 6, slots).transpose(1, 0, 2).reshape(6, n_col * slots)
    ).astype(jnp.float32)
    planes = got[:, 6 * slots :].reshape(n_col, ext_z, BX * y_block)
    spill = jnp.roll(planes[:, planes_z:], 1, axis=0).astype(jnp.float32)
    top = (planes[:, :3].astype(jnp.float32) + spill).astype(jnp.bfloat16)
    pencil = jnp.concatenate([top, planes[:, 3:planes_z]], axis=1).reshape(GZ, BX * y_block)
    norm_scale = 1.0 / jnp.sqrt(jnp.float32(GZ))
    signs = jnp.array([norm_scale, -norm_scale], jnp.float32)[:, None, None]
    table = dft_table().reshape(GZ, 2, GZ).transpose(1, 0, 2) * signs
    table_hi = table.astype(jnp.bfloat16)
    table_lo = (table - table_hi.astype(jnp.float32)).astype(jnp.bfloat16)
    pair = jnp.broadcast_to(pencil[None], (2,) + pencil.shape)
    dims = (((1,), (1,)), ((0,), (0,)))
    spectrum = lax.dot_general(
        pair, table_hi, dims, preferred_element_type=jnp.float32
    ) + lax.dot_general(pair, table_lo, dims, preferred_element_type=jnp.float32)
    spectrum = spectrum.reshape(2, BX, y_block, GZ)
    return (arrived_feat, arrived_state, spectrum)


def dft_table():
    coarse = GZ // 32
    z = jnp.arange(GZ, dtype=jnp.int32)[:, None]
    step = 2.0 * jnp.pi / GZ
    hi_angle = step * ((z * (32 * jnp.arange(coarse, dtype=jnp.int32)[None, :])) % GZ).astype(jnp.float32)
    lo_angle = step * ((z * jnp.arange(32, dtype=jnp.int32)[None, :]) % GZ).astype(jnp.float32)
    ca, sa = jnp.cos(hi_angle)[:, :, None], jnp.sin(hi_angle)[:, :, None]
    cb, sb = jnp.cos(lo_angle)[:, None, :], jnp.sin(lo_angle)[:, None, :]
    cos_t = (ca * cb - sa * sb).reshape(GZ, GZ)
    sin_t = (sa * cb + ca * sb).reshape(GZ, GZ)
    return jnp.concatenate([cos_t, sin_t], axis=1)


def solution(mesh):
    in_specs = (
        P(("row", "col"), None),
        P(None, ("row", "col")),
        P(None, ("row", "col")),
        P(None, ("row", "col")),
        P(("row", "col")),
        P(None, ("row", "col")),
        P(None, ("row", "col")),
        P(("row", "col"), None),
        P(),
        P(),
        P(),
    )
    out_specs = (P(("row", "col"), None), P(None, ("row", "col")), P(None, "row", "col", None))
    return jax.shard_map(body, mesh=mesh, in_specs=in_specs, out_specs=out_specs, check_vma=False)
```

```python
import jax
import jax.numpy as jnp
from jax import lax
from jax.sharding import PartitionSpec as P

BX = 32
GY = 512
GZ = 512


def from_behind(shard, axis, by):
    count = lax.axis_size(axis)
    return lax.ppermute(shard, axis, [(i, (i + by) % count) for i in range(count)])


def bspline(u):
    u2 = u * u
    u3 = u2 * u
    w0 = (1.0 - u) * (1.0 - u) * (1.0 - u) / 6.0
    w1 = (3.0 * u3 - 6.0 * u2 + 4.0) / 6.0
    w2 = (-3.0 * u3 + 3.0 * u2 + 3.0 * u + 1.0) / 6.0
    w3 = u3 / 6.0
    return jnp.stack([w0, w1, w2, w3])


def spline_rows(base, weights, width, wrap):
    columns = jnp.arange(width, dtype=jnp.int32)[None, :]
    total = jnp.zeros((base.shape[0], width), jnp.float32)
    for shift_k in range(4):
        place = base + shift_k
        if wrap:
            place = place % width
        total = total + weights[shift_k][:, None] * (place[:, None] == columns).astype(jnp.float32)
    return total


def dest_rank(target, n_col, block):
    atoms = target.shape[0]
    groups = atoms // block
    onehot = (target[:, None] == jnp.arange(n_col, dtype=jnp.int32)[None, :]).astype(jnp.bfloat16)
    grouped = onehot.reshape(groups, block, n_col)
    lower = (
        jnp.arange(block, dtype=jnp.int32)[:, None] >= jnp.arange(block, dtype=jnp.int32)[None, :]
    ).astype(jnp.bfloat16)
    within = jnp.einsum("ij,gjd->gid", lower, grouped, preferred_element_type=jnp.float32)
    totals = within[:, block - 1, :].astype(jnp.bfloat16)
    before = (
        jnp.arange(groups, dtype=jnp.int32)[:, None] > jnp.arange(groups, dtype=jnp.int32)[None, :]
    ).astype(jnp.bfloat16)
    offsets = jnp.dot(before, totals, preferred_element_type=jnp.float32)
    counted = (within + offsets[:, None, :]) * grouped.astype(jnp.float32)
    rank = jnp.sum(counted, axis=2).reshape(atoms).astype(jnp.int32) - 1
    return onehot, rank


def feature_hidden(feat, w_in):
    return jax.nn.silu(jnp.dot(feat, w_in, preferred_element_type=jnp.float32)).astype(jnp.bfloat16)


def body(features, position, velocity, noise, charge, frac, cell, dest, w_in, w_out, w_force):
    n_col = lax.axis_size("col")
    row_id = lax.axis_index("row")
    col_id = lax.axis_index("col")
    atoms = features.shape[0]
    width = features.shape[1]
    slots = 2 * atoms // n_col
    target = dest[:, 0]
    onehot, rank = dest_rank(target, n_col, 256)
    slot = target * slots + rank
    feat_buf = (
        jnp.zeros((n_col * slots, width), jnp.bfloat16)
        .at[slot]
        .set(features, unique_indices=True, mode="promise_in_bounds")
        .reshape(n_col, slots, width)
    )
    feat_buf, features, rank, onehot, charge, frac, cell = lax.optimization_barrier(
        (feat_buf, features, rank, onehot, charge, frac, cell)
    )
    got_feat = lax.all_to_all(feat_buf, "col", split_axis=0, concat_axis=0, tiled=True)
    hidden = feature_hidden(features, w_in)
    force = lax.dot_general(
        w_force, hidden, (((1,), (1,)), ((), ())), preferred_element_type=jnp.float32
    )
    new_vel = 0.8 * velocity + 0.5 * force + 0.6 * noise
    state = jnp.concatenate([position + 0.5 * new_vel, new_vel], axis=0)
    rank_hot = (rank[:, None] == jnp.arange(slots, dtype=jnp.int32)[None, :]).astype(jnp.bfloat16)
    state_lhs = state.astype(jnp.bfloat16)[:, None, :] * onehot.T[None, :, :]
    state_buf = jnp.dot(
        state_lhs.reshape(6 * n_col, atoms), rank_hot, preferred_element_type=jnp.float32
    ).astype(jnp.bfloat16).reshape(6, n_col, slots)
    planes_z = GZ // n_col
    ext_x = BX + 3
    ext_z = planes_z + 3
    local_x = cell[0] - row_id * BX
    local_y = cell[1]
    local_z = cell[2] - col_id * planes_z
    wx = bspline(frac[0])
    wy = bspline(frac[1])
    wz = bspline(frac[2])
    block = atoms
    extended = jnp.zeros((ext_z * ext_x, GY), jnp.float32)
    for start in range(0, atoms, block):
        stop = start + block
        rows_x = spline_rows(local_x[start:stop], wx[:, start:stop], ext_x, False)
        rows_y = spline_rows(local_y[start:stop], wy[:, start:stop], GY, True)
        rows_z = spline_rows(local_z[start:stop], wz[:, start:stop], ext_z, False)
        kron = (
            charge[start:stop][:, None, None] * rows_z[:, :, None] * rows_x[:, None, :]
        ).reshape(block, ext_z * ext_x)
        extended = extended + lax.dot_general(
            kron,
            rows_y,
            (((0,), (0,)), ((), ())),
            precision=lax.Precision.HIGH,
            preferred_element_type=jnp.float32,
        )
    extended = extended.reshape(ext_z, ext_x, GY)
    from_below = from_behind(extended[:, BX:, :].astype(jnp.bfloat16), "row", 1).astype(jnp.float32)
    slab = extended[:, :BX, :].at[:, :3, :].add(from_below)
    brick = slab.astype(jnp.bfloat16)
    y_block = GY // n_col
    state_part = state_buf.transpose(1, 0, 2).reshape(n_col, 6 * slots)
    grid_part = (
        brick.reshape(ext_z, BX, n_col, y_block).transpose(2, 0, 1, 3).reshape(n_col, -1)
    )
    send = jnp.concatenate(
        [state_part.reshape(n_col, 6, slots), grid_part.reshape(n_col, ext_z, BX * y_block)], axis=1
    )
    send, got_feat = lax.optimization_barrier((send, got_feat))
    got = lax.all_to_all(send, "col", split_axis=0, concat_axis=0, tiled=True)
    arrived = got_feat.reshape(n_col * slots, width)
    arrived_hidden = feature_hidden(arrived, w_in)
    arrived_feat = (
        arrived.astype(jnp.float32)
        + jnp.dot(arrived_hidden, w_out, preferred_element_type=jnp.float32)
    ).astype(jnp.bfloat16)
    arrived_state = (
        got[:, :6].transpose(1, 0, 2).reshape(6, n_col * slots)
    ).astype(jnp.float32)
    planes = got[:, 6:]
    spill = jnp.roll(planes[:, planes_z:], 1, axis=0).astype(jnp.float32)
    top = (planes[:, :3].astype(jnp.float32) + spill).astype(jnp.bfloat16)
    pencil = jnp.concatenate([top, planes[:, 3:planes_z]], axis=1).reshape(GZ, BX * y_block)
    table = dft_table()
    table_hi = table.astype(jnp.bfloat16)
    table_lo = (table - table_hi.astype(jnp.float32)).astype(jnp.bfloat16)
    dims = (((0,), (0,)), ((), ()))
    both = lax.dot_general(
        pencil, table_hi, dims, preferred_element_type=jnp.float32
    ) + lax.dot_general(pencil, table_lo, dims, preferred_element_type=jnp.float32)
    norm_scale = 1.0 / jnp.sqrt(jnp.float32(GZ))
    both = both.reshape(BX, y_block, 2 * GZ)
    real_part = both[..., :GZ] * norm_scale
    imag_part = -both[..., GZ:] * norm_scale
    spectrum = jnp.stack([real_part, imag_part])
    return (arrived_feat, arrived_state, spectrum)


def dft_table():
    coarse = GZ // 32
    z = jnp.arange(GZ, dtype=jnp.int32)[:, None]
    step = 2.0 * jnp.pi / GZ
    hi_angle = step * ((z * (32 * jnp.arange(coarse, dtype=jnp.int32)[None, :])) % GZ).astype(jnp.float32)
    lo_angle = step * ((z * jnp.arange(32, dtype=jnp.int32)[None, :]) % GZ).astype(jnp.float32)
    ca, sa = jnp.cos(hi_angle)[:, :, None], jnp.sin(hi_angle)[:, :, None]
    cb, sb = jnp.cos(lo_angle)[:, None, :], jnp.sin(lo_angle)[:, None, :]
    cos_t = (ca * cb - sa * sb).reshape(GZ, GZ)
    sin_t = (sa * cb + ca * sb).reshape(GZ, GZ)
    return jnp.concatenate([cos_t, sin_t], axis=1)


def solution(mesh):
    in_specs = (
        P(("row", "col"), None),
        P(None, ("row", "col")),
        P(None, ("row", "col")),
        P(None, ("row", "col")),
        P(("row", "col")),
        P(None, ("row", "col")),
        P(None, ("row", "col")),
        P(("row", "col"), None),
        P(),
        P(),
        P(),
    )
    out_specs = (P(("row", "col"), None), P(None, ("row", "col")), P(None, "row", "col", None))
    return jax.shard_map(body, mesh=mesh, in_specs=in_specs, out_specs=out_specs, check_vma=False)
```
